1024 devices in a mesh: ta: 64 (over z, core), gz: 16 (over y, x).
Axes of the slice: x: 4, y: 4, z: 32, core: 2. Of those that a mesh axis runs over, the one named last changes fastest.
Arguments:
- source: bfloat16 [2, 4, 3, 64, 64, 512], P(None, None, None, 'ta', 'gz'), may hold values from -6 to 6
- gauge_links: bfloat16 [4, 2, 3, 3, 64, 64, 512], P(None, None, None, None, 'ta', 'gz'), may hold values from -2.5 to 2.5
- clover_diag: float32 [4, 3, 64, 64, 512], P(None, None, 'ta', 'gz'), may hold values from 0.5 to 4
- agg_map: int32 [64, 64, 512], P('ta', 'gz'), may hold values from 0 to 31
- prolong: bfloat16 [24, 2, 4, 3, 64, 64, 512], P(None, None, None, None, 'ta', 'gz'), may hold values from -0.0390625 to 0.0390625
- coarse_inverse: float32 [64, 768, 768], P('ta', 'gz'), may hold values from -24 to 24
Outputs:
- solution: float32 [2, 4, 3, 64, 64, 512], P(None, None, None, 'ta', 'gz')
The draws below stay inside these ranges and needn't reach their ends.
Inputs may be any that keep to these rules, and one draw needn't show every extreme that they name: `agg_map`: aggregate numbers are local to each group of 16 devices along gz.
All inputs are finite; a program needn't handle non-finite values.
Results may differ from the reference program's by a relative error of at most 0.03.
Values may be sent and summed in bfloat16 or wider, within the bound.
No kernel may reach another device: no remote copies, remote signals or barrier semaphores. Data moves between devices by JAX's collectives and lax.ppermute only.
A program may use at most 32 MiB of HBM per device.

```python
import math
import jax
import jax.numpy as jnp
from jax import lax

LX = 32
LY = 16
TL = 1
NV = 24
NAGG = 32
SITES = 512
T_ALL = 64
Z_ALL = 64
NC = 768
AGG_SITES = 1024
N_TA = 64


def place_ends(values, key, smallest, largest):
    index_at = [jax.random.randint(jax.random.fold_in(key, axis), (), 0, length) for axis, length in enumerate(values.shape)]
    widest = values.shape.index(max(values.shape))
    beside = index_at[:widest] + [(index_at[widest] + 1) % values.shape[widest]] + index_at[widest + 1:]
    return values.at[tuple(index_at)].set(smallest).at[tuple(beside)].set(largest)


def block_scale(own_key, shape, shards, least, largest):
    def one(axis_at, blocks):
        steps = jax.random.uniform(jax.random.fold_in(jax.random.fold_in(own_key, 6), axis_at), (blocks,), jnp.float32, least / len(shards), largest / len(shards))
        return jnp.repeat(jnp.exp(steps), shape[axis_at] // blocks).reshape((-1,) + (1,) * (len(shape) - axis_at - 1))

    level = one(*shards[0])
    for cut in shards[1:]:
        level = level * one(*cut)
    return level


def noise(rng, shape, scale, limit, shards=(), kind=jnp.bfloat16):
    array = scale * jax.random.normal(rng, shape, jnp.float32)
    if shards:
        array = array * block_scale(rng, shape, shards, -0.22, 0.18)
    return jnp.clip(array, -limit, limit).astype(kind)


def setup_inputs(seed: int = 0) -> dict:
    arg_keys = jax.random.split(jax.random.key(seed), 7)
    return {
        "source": noise(arg_keys[0], (2, 4, 3, T_ALL, Z_ALL, SITES), 1.0, 6.0, ((3, 64), (4, 16))),
        "gauge_links": noise(arg_keys[1], (4, 2, 3, 3, T_ALL, Z_ALL, SITES), 6 ** -0.5, 2.5, ((4, 64), (5, 16))),
        "clover_diag": jnp.clip(jnp.exp(math.log(4.0) - 2.0794415 * jax.random.uniform(arg_keys[2], (4, 3, T_ALL, Z_ALL, SITES), jnp.float32) ** block_scale(arg_keys[2], (4, 3, T_ALL, Z_ALL, SITES), ((2, 64), (3, 16)), -0.2, 0.2)), 0.5, 4.0),
        "agg_map": place_ends(jax.random.randint(arg_keys[3], (T_ALL, Z_ALL, SITES), 0, NAGG), jax.random.fold_in(arg_keys[3], 1), 0, NAGG - 1).astype(jnp.int32),
        "prolong": noise(arg_keys[4], (NV, 2, 4, 3, T_ALL, Z_ALL, SITES), (24 * AGG_SITES) ** -0.5, 0.0390625, ((4, 64), (5, 16))),
        "coarse_inverse": noise(arg_keys[5], (N_TA, NC, NC), (3 * (AGG_SITES // NC + 1) ** 0.5), 24.0, ((0, 64), (1, 16)), jnp.float32),
    }


mass_shift = -0.4
spin_perms = ((3, 2, 1, 0), (3, 2, 1, 0), (2, 3, 0, 1), (2, 3, 0, 1))
spin_real = ((0.0, 0.0, 0.0, 0.0), (-1.0, 1.0, 1.0, -1.0), (0.0, 0.0, 0.0, 0.0), (1.0, 1.0, 1.0, 1.0))
spin_imag = ((-1.0, -1.0, 1.0, 1.0), (0.0, 0.0, 0.0, 0.0), (-1.0, 1.0, 1.0, -1.0), (0.0, 0.0, 0.0, 0.0))


def phase_mul(coef_re, coef_im, value_re, value_im):
    if coef_im == 0.0:
        return coef_re * value_re, coef_re * value_im
    return -coef_im * value_im, coef_im * value_re


def project(wide, direction, sign):
    rows_re = []
    rows_im = []
    for slot in range(2):
        other = spin_perms[direction][slot]
        term_re, term_im = phase_mul(spin_real[direction][slot], spin_imag[direction][slot], wide[0, other], wide[1, other])
        rows_re.append(wide[0, slot] + sign * term_re)
        rows_im.append(wide[1, slot] + sign * term_im)
    return jnp.stack([jnp.stack(rows_re), jnp.stack(rows_im)])


def expand(half, direction, sign):
    rows_re = [None] * 4
    rows_im = [None] * 4
    for slot in range(2):
        other = spin_perms[direction][slot]
        rows_re[slot] = half[0, slot]
        rows_im[slot] = half[1, slot]
        term_re, term_im = phase_mul(spin_real[direction][other], spin_imag[direction][other], half[0, slot], half[1, slot])
        rows_re[other] = sign * term_re
        rows_im[other] = sign * term_im
    return jnp.stack([jnp.stack(rows_re), jnp.stack(rows_im)])


def color_mix(link_pair, spinor, dagger):
    link_re = link_pair[0].astype(jnp.float32)
    link_im = link_pair[1].astype(jnp.float32)
    spin_re = spinor[0].astype(jnp.float32)
    spin_im = spinor[1].astype(jnp.float32)
    out_re = []
    out_im = []
    for row in range(3):
        acc_re = None
        acc_im = None
        for col in range(3):
            if dagger:
                entry_re = link_re[col, row]
                entry_im = -link_im[col, row]
            else:
                entry_re = link_re[row, col]
                entry_im = link_im[row, col]
            part_re = entry_re * spin_re[:, col] - entry_im * spin_im[:, col]
            part_im = entry_re * spin_im[:, col] + entry_im * spin_re[:, col]
            acc_re = part_re if acc_re is None else acc_re + part_re
            acc_im = part_im if acc_im is None else acc_im + part_im
        out_re.append(acc_re)
        out_im.append(acc_im)
    return jnp.stack([jnp.stack(out_re, axis=1), jnp.stack(out_im, axis=1)])


def neighbour(values, direction, step):
    if direction == 3:
        return jnp.roll(values, -step, axis=-3)
    if direction == 2:
        return jnp.roll(values, -step, axis=-2)
    dims_all = values.shape
    grid = values.reshape(dims_all[:-1] + (LY, LX))
    rolled = jnp.roll(grid, -step, axis=-1 if direction == 0 else -2)
    return rolled.reshape(dims_all)


def hopping(spinor, gauge_links):
    wide = spinor.astype(jnp.float32)
    total = jnp.zeros(spinor.shape, jnp.float32)
    for direction in range(4):
        fwd_half = lax.optimization_barrier(project(wide, direction, -1.0).astype(jnp.bfloat16))
        ahead = neighbour(fwd_half, direction, 1)
        total = total + expand(color_mix(gauge_links[direction], ahead, False), direction, -1.0)
        back_half = lax.optimization_barrier(project(color_mix(gauge_links[direction], spinor, True), direction, 1.0).astype(jnp.bfloat16))
        behind = neighbour(back_half, direction, -1).astype(jnp.float32)
        total = total + expand(behind, direction, 1.0)
    return total


def reference(source, gauge_links, clover_diag, agg_map, prolong, coarse_inverse):
    hp = lax.Precision.HIGHEST
    diagonal = 4.0 + mass_shift + clover_diag
    source_wide = source.astype(jnp.float32)
    first_iter = source_wide / diagonal
    first_half = first_iter.astype(jnp.bfloat16)
    first_resid = source_wide - diagonal * first_iter + 0.5 * hopping(first_half, gauge_links)
    second_iter = first_iter + first_resid / diagonal
    second_half = second_iter.astype(jnp.bfloat16)
    second_resid = source_wide - diagonal * second_iter + 0.5 * hopping(second_half, gauge_links)
    resid_half = second_resid.astype(jnp.bfloat16)
    labels = jnp.arange(NAGG, dtype=jnp.int32)

    def restrict_slice(slice_index):
        prolong_slice = lax.dynamic_index_in_dim(prolong, slice_index, 4, keepdims=False).astype(jnp.float32)
        resid_slice = lax.dynamic_index_in_dim(resid_half, slice_index, 3, keepdims=False).astype(jnp.float32)
        map_slice = lax.dynamic_index_in_dim(agg_map, slice_index, 0, keepdims=False)
        projected = jnp.einsum("vrsczn,rsczn->vzn", prolong_slice, resid_slice, precision=hp)
        member = (map_slice.reshape(-1)[None, :] == labels[:, None]).astype(jnp.float32)
        return jnp.einsum("am,vm->av", member, projected.reshape(NV, -1), precision=hp)

    partial_all = lax.map(restrict_slice, jnp.arange(T_ALL, dtype=jnp.int32))
    coarse_resid = partial_all.reshape(N_TA, TL, NC).sum(axis=1)
    correction = jnp.einsum("gij,gj->gi", coarse_inverse, coarse_resid, precision=hp)
    correction_half = correction.astype(jnp.bfloat16)

    def prolong_slice_fn(slice_index):
        group_index = slice_index // TL
        prolong_slice = lax.dynamic_index_in_dim(prolong, slice_index, 4, keepdims=False).astype(jnp.float32)
        map_slice = lax.dynamic_index_in_dim(agg_map, slice_index, 0, keepdims=False)
        values_here = lax.dynamic_index_in_dim(correction_half, group_index, 0, keepdims=False).astype(jnp.float32).reshape(NAGG, NV)
        member = (map_slice.reshape(-1)[None, :] == labels[:, None]).astype(jnp.float32)
        spread = jnp.einsum("av,am->vm", values_here, member, precision=hp).reshape(NV, Z_ALL, SITES)
        return jnp.einsum("vrsczn,vzn->rsczn", prolong_slice, spread, precision=hp)

    smooth = lax.map(prolong_slice_fn, jnp.arange(T_ALL, dtype=jnp.int32))
    return second_iter + jnp.moveaxis(smooth, 0, 3)
```

```python
import jax
import jax.numpy as jnp
from jax import lax
from jax.sharding import Mesh, PartitionSpec as P

LX = 32
LY = 16
NAGG = 32


mass_shift = -0.4
spin_perms = ((3, 2, 1, 0), (3, 2, 1, 0), (2, 3, 0, 1), (2, 3, 0, 1))
spin_real = (
    (0.0, 0.0, 0.0, 0.0),
    (-1.0, 1.0, 1.0, -1.0),
    (0.0, 0.0, 0.0, 0.0),
    (1.0, 1.0, 1.0, 1.0),
)
spin_imag = (
    (-1.0, -1.0, 1.0, 1.0),
    (0.0, 0.0, 0.0, 0.0),
    (-1.0, 1.0, 1.0, -1.0),
    (0.0, 0.0, 0.0, 0.0),
)


GZ = ("gy", "gx")


def shifted(block, axis, distance):
    devices = range(16 if axis == GZ else lax.axis_size(axis))
    route = [((i - distance) % len(devices), i) for i in devices]
    return lax.ppermute(block, axis, route)


def phase_mul(coef_re, coef_im, value_re, value_im):
    if coef_im == 0.0:
        return (coef_re * value_re, coef_re * value_im)
    return (-coef_im * value_im, coef_im * value_re)


def project(wide, direction, sign):
    rows_re = []
    rows_im = []
    for slot in range(2):
        other = spin_perms[direction][slot]
        term_re, term_im = phase_mul(
            spin_real[direction][slot], spin_imag[direction][slot], wide[0, other], wide[1, other]
        )
        rows_re.append(wide[0, slot] + sign * term_re)
        rows_im.append(wide[1, slot] + sign * term_im)
    return jnp.stack([jnp.stack(rows_re), jnp.stack(rows_im)])


def expand(half, direction, sign):
    rows_re = [None] * 4
    rows_im = [None] * 4
    for slot in range(2):
        other = spin_perms[direction][slot]
        rows_re[slot] = half[0, slot]
        rows_im[slot] = half[1, slot]
        term_re, term_im = phase_mul(
            spin_real[direction][other], spin_imag[direction][other], half[0, slot], half[1, slot]
        )
        rows_re[other] = sign * term_re
        rows_im[other] = sign * term_im
    return jnp.stack([jnp.stack(rows_re), jnp.stack(rows_im)])


def color_mix(link_pair, spinor, dagger):
    link_re = link_pair[0].astype(jnp.float32)
    link_im = link_pair[1].astype(jnp.float32)
    spin_re = spinor[0].astype(jnp.float32)
    spin_im = spinor[1].astype(jnp.float32)
    out_re = []
    out_im = []
    for row in range(3):
        acc_re = None
        acc_im = None
        for col in range(3):
            if dagger:
                entry_re = link_re[col, row]
                entry_im = -link_im[col, row]
            else:
                entry_re = link_re[row, col]
                entry_im = link_im[row, col]
            part_re = entry_re * spin_re[:, col] - entry_im * spin_im[:, col]
            part_im = entry_re * spin_im[:, col] + entry_im * spin_re[:, col]
            acc_re = part_re if acc_re is None else acc_re + part_re
            acc_im = part_im if acc_im is None else acc_im + part_im
        out_re.append(acc_re)
        out_im.append(acc_im)
    return jnp.stack([jnp.stack(out_re, axis=1), jnp.stack(out_im, axis=1)])


def local_shift(values, direction, step):
    dims_all = values.shape
    grid = values.reshape(dims_all[:-1] + (LY, LX))
    rolled = jnp.roll(grid, -step, axis=-1 if direction == 0 else -2)
    return rolled.reshape(dims_all)


def fwd_round(wide, direction):
    return lax.optimization_barrier(project(wide, direction, -1.0).astype(jnp.bfloat16))


def hopping(spinor, gauge_links):
    wide = spinor.astype(jnp.float32)
    total = jnp.zeros(spinor.shape, jnp.float32)
    back_space = lax.optimization_barrier(
        project(color_mix(gauge_links[2], spinor, True), 2, 1.0).astype(jnp.bfloat16)
    )
    back_time = lax.optimization_barrier(
        project(color_mix(gauge_links[3], spinor, True), 3, 1.0).astype(jnp.bfloat16)
    )
    send_bz = expand(back_space.astype(jnp.float32), 2, 1.0).astype(jnp.bfloat16)
    send_bt = expand(back_time.astype(jnp.float32), 3, 1.0).astype(jnp.bfloat16)
    ahead_time = shifted(spinor, "ta", -1)
    fwd_time = jnp.concatenate([spinor[:, :, :, 1:], ahead_time], axis=3)
    behind_time = shifted(send_bt, "ta", 1)
    bwd_time = jnp.concatenate([behind_time, send_bt[:, :, :, :-1]], axis=3)
    ahead_space = shifted(spinor[:, :, :, :, 0:1], GZ, -1)
    fwd_space = jnp.concatenate([spinor[:, :, :, :, 1:], ahead_space], axis=4)
    behind_space = shifted(send_bz[:, :, :, :, -1:], GZ, 1)
    bwd_space = jnp.concatenate([behind_space, send_bz[:, :, :, :, :-1]], axis=4)
    fwd_space = fwd_round(fwd_space.astype(jnp.float32), 2)
    fwd_time = fwd_round(fwd_time.astype(jnp.float32), 3)
    bwd_space = bwd_space[:, 0:2]
    bwd_time = bwd_time[:, 0:2]
    for direction in range(2):
        ahead = local_shift(fwd_round(wide, direction), direction, 1)
        total = total + expand(color_mix(gauge_links[direction], ahead, False), direction, -1.0)
        back_half = lax.optimization_barrier(
            project(color_mix(gauge_links[direction], spinor, True), direction, 1.0).astype(
                jnp.bfloat16
            )
        )
        behind = local_shift(back_half, direction, -1).astype(jnp.float32)
        total = total + expand(behind, direction, 1.0)
    total = total + expand(color_mix(gauge_links[2], fwd_space, False), 2, -1.0)
    total = total + expand(bwd_space.astype(jnp.float32), 2, 1.0)
    total = total + expand(color_mix(gauge_links[3], fwd_time, False), 3, -1.0)
    total = total + expand(bwd_time.astype(jnp.float32), 3, 1.0)
    return total


def shards(source, gauge_links, clover_diag, agg_map, prolong, coarse_inverse):
    highest = lax.Precision.HIGHEST
    diagonal = 4.0 + mass_shift + clover_diag
    source_wide = source.astype(jnp.float32)
    first_iter = source_wide / diagonal
    first_half = first_iter.astype(jnp.bfloat16)
    first_resid = source_wide - diagonal * first_iter + 0.5 * hopping(first_half, gauge_links)
    second_iter = first_iter + first_resid / diagonal
    second_half = second_iter.astype(jnp.bfloat16)
    second_resid = source_wide - diagonal * second_iter + 0.5 * hopping(second_half, gauge_links)
    resid_half = second_resid.astype(jnp.bfloat16)
    projected = jnp.einsum(
        "vrsctzn,rsctzn->vtzn", prolong, resid_half, preferred_element_type=jnp.float32
    )
    vectors = prolong.shape[0]
    labels = jnp.arange(NAGG, dtype=jnp.int32)
    member = agg_map.reshape(-1)[None, :] == labels[:, None]
    partial_sum = jnp.einsum(
        "am,vm->av", member.astype(jnp.float32), projected.reshape(vectors, -1), precision=highest
    )
    coarse_resid = lax.psum(lax.psum(partial_sum.reshape(-1), "gx"), "gy")
    own_rows = jnp.dot(coarse_inverse[0], coarse_resid, precision=highest)
    rows = own_rows.shape[0]
    place = (lax.axis_index("gy") * 4 + lax.axis_index("gx")) * rows
    padded = lax.dynamic_update_slice(
        jnp.zeros((rows * 16,), jnp.bfloat16), own_rows.astype(jnp.bfloat16), (place,)
    )
    correction_half = lax.psum(lax.psum(padded, "gx"), "gy").reshape(NAGG, vectors)
    spread = jnp.einsum(
        "av,am->vm",
        correction_half,
        member.astype(jnp.bfloat16),
        preferred_element_type=jnp.float32,
    ).astype(jnp.bfloat16)
    smooth = jnp.einsum(
        "vrsctzn,vtzn->rsctzn",
        prolong,
        spread.reshape(projected.shape),
        preferred_element_type=jnp.float32,
    )
    return second_iter + smooth


def solution(mesh):
    ta, gz = mesh.devices.shape
    grid = Mesh(mesh.devices.reshape(ta, 4, gz // 4), ("ta", "gy", "gx"))
    return jax.shard_map(
        shards,
        mesh=grid,
        in_specs=(
            P(None, None, None, "ta", GZ, None),
            P(None, None, None, None, "ta", GZ, None),
            P(None, None, "ta", GZ, None),
            P("ta", GZ, None),
            P(None, None, None, None, "ta", GZ, None),
            P("ta", GZ, None),
        ),
        out_specs=P(None, None, None, "ta", GZ, None),
        check_vma=False,
    )
```

```python
import jax
import jax.numpy as jnp
from jax import lax
from jax.sharding import Mesh, PartitionSpec as P

LX = 32
LY = 16
NAGG = 32


mass_shift = -0.4
spin_perms = ((3, 2, 1, 0), (3, 2, 1, 0), (2, 3, 0, 1), (2, 3, 0, 1))
spin_real = (
    (0.0, 0.0, 0.0, 0.0),
    (-1.0, 1.0, 1.0, -1.0),
    (0.0, 0.0, 0.0, 0.0),
    (1.0, 1.0, 1.0, 1.0),
)
spin_imag = (
    (-1.0, -1.0, 1.0, 1.0),
    (0.0, 0.0, 0.0, 0.0),
    (-1.0, 1.0, 1.0, -1.0),
    (0.0, 0.0, 0.0, 0.0),
)


GZ = ("gy", "gx")


def shifted(block, axis, distance):
    devices = range(16 if axis == GZ else lax.axis_size(axis))
    route = [((i - distance) % len(devices), i) for i in devices]
    return lax.ppermute(block, axis, route)


def phase_mul(coef_re, coef_im, value_re, value_im):
    if coef_im == 0.0:
        return (coef_re * value_re, coef_re * value_im)
    return (-coef_im * value_im, coef_im * value_re)


def project(wide, direction, sign):
    rows_re = []
    rows_im = []
    for slot in range(2):
        other = spin_perms[direction][slot]
        term_re, term_im = phase_mul(
            spin_real[direction][slot], spin_imag[direction][slot], wide[0, other], wide[1, other]
        )
        rows_re.append(wide[0, slot] + sign * term_re)
        rows_im.append(wide[1, slot] + sign * term_im)
    return jnp.stack([jnp.stack(rows_re), jnp.stack(rows_im)])


def expand(half, direction, sign):
    rows_re = [None] * 4
    rows_im = [None] * 4
    for slot in range(2):
        other = spin_perms[direction][slot]
        rows_re[slot] = half[0, slot]
        rows_im[slot] = half[1, slot]
        term_re, term_im = phase_mul(
            spin_real[direction][other], spin_imag[direction][other], half[0, slot], half[1, slot]
        )
        rows_re[other] = sign * term_re
        rows_im[other] = sign * term_im
    return jnp.stack([jnp.stack(rows_re), jnp.stack(rows_im)])


def color_mix(link_pair, spinor, dagger):
    link_re = link_pair[0].astype(jnp.float32)
    link_im = link_pair[1].astype(jnp.float32)
    spin_re = spinor[0].astype(jnp.float32)
    spin_im = spinor[1].astype(jnp.float32)
    out_re = []
    out_im = []
    for row in range(3):
        acc_re = None
        acc_im = None
        for col in range(3):
            if dagger:
                entry_re = link_re[col, row]
                entry_im = -link_im[col, row]
            else:
                entry_re = link_re[row, col]
                entry_im = link_im[row, col]
            part_re = entry_re * spin_re[:, col] - entry_im * spin_im[:, col]
            part_im = entry_re * spin_im[:, col] + entry_im * spin_re[:, col]
            acc_re = part_re if acc_re is None else acc_re + part_re
            acc_im = part_im if acc_im is None else acc_im + part_im
        out_re.append(acc_re)
        out_im.append(acc_im)
    return jnp.stack([jnp.stack(out_re, axis=1), jnp.stack(out_im, axis=1)])


def local_shift(values, direction, step):
    if direction == 1:
        return jnp.roll(values, -step * LX, axis=-1)
    column = lax.broadcasted_iota(jnp.int32, values.shape, values.ndim - 1) % LX
    edge = LX - 1 if step > 0 else 0
    return jnp.where(
        column == edge,
        jnp.roll(values, step * (LX - 1), axis=-1),
        jnp.roll(values, -step, axis=-1),
    )


def halo(block, axis, dim, step):
    size = block.shape[dim]
    if step > 0:
        edge = lax.slice_in_dim(block, 0, 1, axis=dim)
        inner = lax.slice_in_dim(block, 1, size, axis=dim)
        return jnp.concatenate([inner, shifted(edge, axis, -1)], axis=dim)
    edge = lax.slice_in_dim(block, size - 1, size, axis=dim)
    inner = lax.slice_in_dim(block, 0, size - 1, axis=dim)
    return jnp.concatenate([shifted(edge, axis, 1), inner], axis=dim)


def hopping(spinor, gauge_links):
    wide = spinor.astype(jnp.float32)
    fwd = [project(wide, mu, -1.0).astype(jnp.bfloat16) for mu in range(4)]
    back = [
        project(color_mix(gauge_links[mu], spinor, True), mu, 1.0).astype(jnp.bfloat16)
        for mu in range(4)
    ]
    ahead = [local_shift(fwd[0], 0, 1), local_shift(fwd[1], 1, 1)]
    behind = [local_shift(back[0], 0, -1), local_shift(back[1], 1, -1)]
    ahead += [halo(fwd[2], GZ, 4, 1), halo(fwd[3], "ta", 3, 1)]
    behind += [halo(back[2], GZ, 4, -1), halo(back[3], "ta", 3, -1)]
    total = None
    for mu in range(4):
        term = expand(color_mix(gauge_links[mu], ahead[mu], False), mu, -1.0)
        term = term + expand(behind[mu].astype(jnp.float32), mu, 1.0)
        total = term if total is None else total + term
    return total


def shards(source, gauge_links, clover_diag, agg_map, prolong, coarse_inverse):
    highest = lax.Precision.HIGHEST
    diagonal = 4.0 + mass_shift + clover_diag
    source_wide = source.astype(jnp.float32)
    first_iter = source_wide / diagonal
    first_half = first_iter.astype(jnp.bfloat16)
    first_resid = source_wide - diagonal * first_iter + 0.5 * hopping(first_half, gauge_links)
    second_iter = first_iter + first_resid / diagonal
    second_half = second_iter.astype(jnp.bfloat16)
    second_resid = source_wide - diagonal * second_iter + 0.5 * hopping(second_half, gauge_links)
    resid_half = second_resid.astype(jnp.bfloat16)
    projected = jnp.einsum(
        "vrsctzn,rsctzn->vtzn", prolong, resid_half, preferred_element_type=jnp.float32
    )
    vectors = prolong.shape[0]
    labels = jnp.arange(NAGG, dtype=jnp.int32)
    member = agg_map.reshape(-1)[None, :] == labels[:, None]
    partial_sum = jnp.einsum(
        "am,vm->av", member.astype(jnp.float32), projected.reshape(vectors, -1), precision=highest
    )
    coarse_resid = lax.psum(lax.psum(partial_sum.reshape(-1), "gx"), "gy")
    own_rows = jnp.dot(coarse_inverse[0], coarse_resid, precision=highest)
    rows = own_rows.shape[0]
    place = (lax.axis_index("gy") * 4 + lax.axis_index("gx")) * rows
    padded = lax.dynamic_update_slice(
        jnp.zeros((rows * 16,), jnp.bfloat16), own_rows.astype(jnp.bfloat16), (place,)
    )
    correction_half = lax.psum(lax.psum(padded, "gx"), "gy").reshape(NAGG, vectors)
    spread = jnp.einsum(
        "av,am->vm",
        correction_half,
        member.astype(jnp.bfloat16),
        preferred_element_type=jnp.float32,
    ).astype(jnp.bfloat16)
    smooth = jnp.einsum(
        "vrsctzn,vtzn->rsctzn",
        prolong,
        spread.reshape(projected.shape),
        preferred_element_type=jnp.float32,
    )
    return second_iter + smooth


def solution(mesh):
    ta, gz = mesh.devices.shape
    grid = Mesh(mesh.devices.reshape(ta, 4, gz // 4), ("ta", "gy", "gx"))
    return jax.shard_map(
        shards,
        mesh=grid,
        in_specs=(
            P(None, None, None, "ta", GZ, None),
            P(None, None, None, None, "ta", GZ, None),
            P(None, None, "ta", GZ, None),
            P("ta", GZ, None),
            P(None, None, None, None, "ta", GZ, None),
            P("ta", GZ, None),
        ),
        out_specs=P(None, None, None, "ta", GZ, None),
        check_vma=False,
    )
```

```python
import jax
import jax.numpy as jnp
from jax import lax
from jax.experimental import pallas as pl
from jax.experimental.pallas import tpu as pltpu
from jax.sharding import Mesh, PartitionSpec as P

LX = 32
LY = 16
NAGG = 32


mass_shift = -0.4
spin_perms = ((3, 2, 1, 0), (3, 2, 1, 0), (2, 3, 0, 1), (2, 3, 0, 1))
spin_real = (
    (0.0, 0.0, 0.0, 0.0),
    (-1.0, 1.0, 1.0, -1.0),
    (0.0, 0.0, 0.0, 0.0),
    (1.0, 1.0, 1.0, 1.0),
)
spin_imag = (
    (-1.0, -1.0, 1.0, 1.0),
    (0.0, 0.0, 0.0, 0.0),
    (-1.0, 1.0, 1.0, -1.0),
    (0.0, 0.0, 0.0, 0.0),
)


GZ = ("gy", "gx")


def shifted(block, axis, distance):
    count = 1
    for name in axis if isinstance(axis, tuple) else (axis,):
        count *= lax.axis_size(name)
    devices = range(count)
    route = [((i - distance) % len(devices), i) for i in devices]
    return lax.ppermute(block, axis, route)


def phase_mul(coef_re, coef_im, value_re, value_im):
    if coef_im == 0.0:
        return (coef_re * value_re, coef_re * value_im)
    return (-coef_im * value_im, coef_im * value_re)


def project(wide, direction, sign):
    rows_re = []
    rows_im = []
    for slot in range(2):
        other = spin_perms[direction][slot]
        term_re, term_im = phase_mul(
            spin_real[direction][slot], spin_imag[direction][slot], wide[0, other], wide[1, other]
        )
        rows_re.append(wide[0, slot] + sign * term_re)
        rows_im.append(wide[1, slot] + sign * term_im)
    return jnp.stack([jnp.stack(rows_re), jnp.stack(rows_im)])


def expand(half, direction, sign):
    rows_re = [None] * 4
    rows_im = [None] * 4
    for slot in range(2):
        other = spin_perms[direction][slot]
        rows_re[slot] = half[0, slot]
        rows_im[slot] = half[1, slot]
        term_re, term_im = phase_mul(
            spin_real[direction][other], spin_imag[direction][other], half[0, slot], half[1, slot]
        )
        rows_re[other] = sign * term_re
        rows_im[other] = sign * term_im
    return jnp.stack([jnp.stack(rows_re), jnp.stack(rows_im)])


def color_mix(link_pair, spinor, dagger):
    link_re = link_pair[0].astype(jnp.float32)
    link_im = link_pair[1].astype(jnp.float32)
    spin_re = spinor[0].astype(jnp.float32)
    spin_im = spinor[1].astype(jnp.float32)
    out_re = []
    out_im = []
    for row in range(3):
        acc_re = None
        acc_im = None
        for col in range(3):
            if dagger:
                entry_re = link_re[col, row]
                entry_im = -link_im[col, row]
            else:
                entry_re = link_re[row, col]
                entry_im = link_im[row, col]
            part_re = entry_re * spin_re[:, col] - entry_im * spin_im[:, col]
            part_im = entry_re * spin_im[:, col] + entry_im * spin_re[:, col]
            acc_re = part_re if acc_re is None else acc_re + part_re
            acc_im = part_im if acc_im is None else acc_im + part_im
        out_re.append(acc_re)
        out_im.append(acc_im)
    return jnp.stack([jnp.stack(out_re, axis=1), jnp.stack(out_im, axis=1)])


def local_shift(values, direction, step):
    if direction == 1:
        return jnp.roll(values, -step * LX, axis=-1)
    column = lax.broadcasted_iota(jnp.int32, values.shape, values.ndim - 1) % LX
    edge = LX - 1 if step > 0 else 0
    return jnp.where(
        column == edge,
        jnp.roll(values, step * (LX - 1), axis=-1),
        jnp.roll(values, -step, axis=-1),
    )


def halo(block, axis, dim, step):
    size = block.shape[dim]
    if step > 0:
        edge = lax.slice_in_dim(block, 0, 1, axis=dim)
        inner = lax.slice_in_dim(block, 1, size, axis=dim)
        return jnp.concatenate([inner, shifted(edge, axis, -1)], axis=dim)
    edge = lax.slice_in_dim(block, size - 1, size, axis=dim)
    inner = lax.slice_in_dim(block, 0, size - 1, axis=dim)
    return jnp.concatenate([shifted(edge, axis, 1), inner], axis=dim)


def nested_project(wide, direction, sign):
    rows = [[], []]
    for slot in range(2):
        other = spin_perms[direction][slot]
        row_re, row_im = [], []
        for color in range(3):
            term_re, term_im = phase_mul(
                spin_real[direction][slot],
                spin_imag[direction][slot],
                wide[0][other][color],
                wide[1][other][color],
            )
            row_re.append(wide[0][slot][color] + sign * term_re)
            row_im.append(wide[1][slot][color] + sign * term_im)
        rows[0].append(row_re)
        rows[1].append(row_im)
    return rows


def nested_expand(half, direction, sign):
    rows = [[None] * 4, [None] * 4]
    for slot in range(2):
        other = spin_perms[direction][slot]
        rows[0][slot] = half[0][slot]
        rows[1][slot] = half[1][slot]
        pairs = [
            phase_mul(
                spin_real[direction][other],
                spin_imag[direction][other],
                half[0][slot][color],
                half[1][slot][color],
            )
            for color in range(3)
        ]
        rows[0][other] = [sign * pair[0] for pair in pairs]
        rows[1][other] = [sign * pair[1] for pair in pairs]
    return rows


def nested_mix(link, spinor, dagger):
    out = [[], []]
    for spin in range(len(spinor[0])):
        out_re, out_im = [], []
        for row in range(3):
            acc_re = None
            acc_im = None
            for col in range(3):
                if dagger:
                    entry_re = link[0][col][row]
                    entry_im = -link[1][col][row]
                else:
                    entry_re = link[0][row][col]
                    entry_im = link[1][row][col]
                spin_re = spinor[0][spin][col]
                spin_im = spinor[1][spin][col]
                part_re = entry_re * spin_re - entry_im * spin_im
                part_im = entry_re * spin_im + entry_im * spin_re
                acc_re = part_re if acc_re is None else acc_re + part_re
                acc_im = part_im if acc_im is None else acc_im + part_im
            out_re.append(acc_re)
            out_im.append(acc_im)
        out[0].append(out_re)
        out[1].append(out_im)
    return out


def nested_map(nested, fn):
    return [[[fn(value) for value in colors] for colors in spins] for spins in nested]


def nested_read(ref, spins):
    return [
        [[ref[(part * spins + spin) * 3 + color].astype(jnp.float32) for color in range(3)] for spin in range(spins)]
        for part in range(2)
    ]


def hop_kernel(v_ref, u_ref, az_ref, bz_ref, at_ref, bt_ref, out_ref):
    width = v_ref.shape[-1]
    wide = nested_read(v_ref, 4)
    column = lax.broadcasted_iota(jnp.int32, wide[0][0][0].shape, 1) % LX

    def link(mu):
        return [
            [[u_ref[mu, (part * 3 + row) * 3 + col].astype(jnp.float32) for col in range(3)] for row in range(3)]
            for part in range(2)
        ]

    def round_half(value):
        return value.astype(jnp.bfloat16).astype(jnp.float32)

    shifts_ahead = (
        lambda a: jnp.where(column == LX - 1, pltpu.roll(a, LX - 1, 1), pltpu.roll(a, width - 1, 1)),
        lambda a: pltpu.roll(a, width - LX, 1),
    )
    shifts_behind = (
        lambda a: jnp.where(column == 0, pltpu.roll(a, width - LX + 1, 1), pltpu.roll(a, 1, 1)),
        lambda a: pltpu.roll(a, LX, 1),
    )
    total = [[[None] * 3 for _ in range(4)] for _ in range(2)]

    def accumulate(term):
        for part in range(2):
            for spin in range(4):
                for color in range(3):
                    value = term[part][spin][color]
                    old = total[part][spin][color]
                    total[part][spin][color] = value if old is None else old + value

    for mu in range(4):
        links = link(mu)
        if mu < 2:
            ahead = nested_map(nested_project(wide, mu, -1.0), lambda a: shifts_ahead[mu](round_half(a)))
            back = nested_project(nested_mix(links, wide, True), mu, 1.0)
            behind = nested_map(back, lambda a: shifts_behind[mu](round_half(a)))
        else:
            ahead = nested_read(az_ref if mu == 2 else at_ref, 2)
            behind = nested_read(bz_ref if mu == 2 else bt_ref, 2)
        accumulate(nested_expand(nested_mix(links, ahead, False), mu, -1.0))
        accumulate(nested_expand(behind, mu, 1.0))
    for part in range(2):
        for spin in range(4):
            for color in range(3):
                out_ref[(part * 4 + spin) * 3 + color] = total[part][spin][color]


def hopping(spinor, gauge_links):
    wide = spinor.astype(jnp.float32)
    fwd_z = project(wide, 2, -1.0).astype(jnp.bfloat16)
    fwd_t = project(wide, 3, -1.0).astype(jnp.bfloat16)
    back_z = project(color_mix(gauge_links[2], spinor, True), 2, 1.0).astype(jnp.bfloat16)
    back_t = project(color_mix(gauge_links[3], spinor, True), 3, 1.0).astype(jnp.bfloat16)
    halves = [
        halo(fwd_z, GZ, 4, 1),
        halo(back_z, GZ, 4, -1),
        halo(fwd_t, "ta", 3, 1),
        halo(back_t, "ta", 3, -1),
    ]
    shape = spinor.shape
    rows = shape[3] * shape[4]
    width = shape[5]
    flat = [half.reshape(12, rows, width) for half in halves]
    links = gauge_links.reshape(4, 18, rows, width)
    total = pl.pallas_call(
        hop_kernel,
        out_shape=jax.ShapeDtypeStruct((24, rows, width), jnp.float32),
        in_specs=[pl.BlockSpec(memory_space=pltpu.VMEM)] * 6,
        out_specs=pl.BlockSpec(memory_space=pltpu.VMEM),
        cost_estimate=pl.CostEstimate(
            flops=24 * 1024 * rows * width // 8, bytes_accessed=2 * 160 * rows * width, transcendentals=0
        ),
    )(spinor.reshape(24, rows, width), links, *flat)
    return total.reshape(shape)


def shards(source, gauge_links, clover_diag, agg_map, prolong, coarse_inverse):
    highest = lax.Precision.HIGHEST
    diagonal = 4.0 + mass_shift + clover_diag
    source_wide = source.astype(jnp.float32)
    first_iter = source_wide / diagonal
    first_half = first_iter.astype(jnp.bfloat16)
    first_resid = source_wide - diagonal * first_iter + 0.5 * hopping(first_half, gauge_links)
    second_iter = first_iter + first_resid / diagonal
    second_half = second_iter.astype(jnp.bfloat16)
    second_resid = source_wide - diagonal * second_iter + 0.5 * hopping(second_half, gauge_links)
    resid_half = second_resid.astype(jnp.bfloat16)
    projected = jnp.einsum(
        "vrsctzn,rsctzn->vtzn", prolong, resid_half, preferred_element_type=jnp.float32
    )
    vectors = prolong.shape[0]
    labels = jnp.arange(NAGG, dtype=jnp.int32)
    member = agg_map.reshape(-1)[None, :] == labels[:, None]
    partial_sum = jnp.einsum(
        "am,vm->av", member.astype(jnp.float32), projected.reshape(vectors, -1), precision=highest
    )
    coarse_resid = lax.psum(lax.psum(partial_sum.reshape(-1), "gx"), "gy")
    own_rows = jnp.dot(coarse_inverse[0], coarse_resid, precision=highest)
    rows = own_rows.shape[0]
    place = (lax.axis_index("gy") * lax.axis_size("gx") + lax.axis_index("gx")) * rows
    padded = lax.dynamic_update_slice(
        jnp.zeros((rows * lax.axis_size("gy") * lax.axis_size("gx"),), jnp.bfloat16), own_rows.astype(jnp.bfloat16), (place,)
    )
    correction_half = lax.psum(lax.psum(padded, "gx"), "gy").reshape(NAGG, vectors)
    spread = jnp.einsum(
        "av,am->vm",
        correction_half,
        member.astype(jnp.bfloat16),
        preferred_element_type=jnp.float32,
    ).astype(jnp.bfloat16)
    smooth = jnp.einsum(
        "vrsctzn,vtzn->rsctzn",
        prolong,
        spread.reshape(projected.shape),
        preferred_element_type=jnp.float32,
    )
    return second_iter + smooth


def solution(mesh):
    ta, gz = mesh.devices.shape
    grid = Mesh(mesh.devices.reshape(ta, 4, gz // 4), ("ta", "gy", "gx"))
    return jax.shard_map(
        shards,
        mesh=grid,
        in_specs=(
            P(None, None, None, "ta", GZ, None),
            P(None, None, None, None, "ta", GZ, None),
            P(None, None, "ta", GZ, None),
            P("ta", GZ, None),
            P(None, None, None, None, "ta", GZ, None),
            P("ta", GZ, None),
        ),
        out_specs=P(None, None, None, "ta", GZ, None),
        check_vma=False,
    )
```

```python
import jax
import jax.numpy as jnp
from jax import lax
from jax.experimental import pallas as pl
from jax.experimental.pallas import tpu as pltpu
from jax.sharding import Mesh, PartitionSpec as P

LX = 32
LY = 16
NAGG = 32


mass_shift = -0.4
spin_perms = ((3, 2, 1, 0), (3, 2, 1, 0), (2, 3, 0, 1), (2, 3, 0, 1))
spin_real = (
    (0.0, 0.0, 0.0, 0.0),
    (-1.0, 1.0, 1.0, -1.0),
    (0.0, 0.0, 0.0, 0.0),
    (1.0, 1.0, 1.0, 1.0),
)
spin_imag = (
    (-1.0, -1.0, 1.0, 1.0),
    (0.0, 0.0, 0.0, 0.0),
    (-1.0, 1.0, 1.0, -1.0),
    (0.0, 0.0, 0.0, 0.0),
)


GZ = ("gy", "gx")


def shifted(block, axis, distance):
    count = 1
    for name in axis if isinstance(axis, tuple) else (axis,):
        count *= lax.axis_size(name)
    devices = range(count)
    route = [((i - distance) % len(devices), i) for i in devices]
    return lax.ppermute(block, axis, route)


def phase_mul(coef_re, coef_im, value_re, value_im):
    if coef_im == 0.0:
        return (coef_re * value_re, coef_re * value_im)
    return (-coef_im * value_im, coef_im * value_re)


def project(wide, direction, sign):
    rows_re = []
    rows_im = []
    for slot in range(2):
        other = spin_perms[direction][slot]
        term_re, term_im = phase_mul(
            spin_real[direction][slot], spin_imag[direction][slot], wide[0, other], wide[1, other]
        )
        rows_re.append(wide[0, slot] + sign * term_re)
        rows_im.append(wide[1, slot] + sign * term_im)
    return jnp.stack([jnp.stack(rows_re), jnp.stack(rows_im)])


def expand(half, direction, sign):
    rows_re = [None] * 4
    rows_im = [None] * 4
    for slot in range(2):
        other = spin_perms[direction][slot]
        rows_re[slot] = half[0, slot]
        rows_im[slot] = half[1, slot]
        term_re, term_im = phase_mul(
            spin_real[direction][other], spin_imag[direction][other], half[0, slot], half[1, slot]
        )
        rows_re[other] = sign * term_re
        rows_im[other] = sign * term_im
    return jnp.stack([jnp.stack(rows_re), jnp.stack(rows_im)])


def color_mix(link_pair, spinor, dagger):
    link_re = link_pair[0].astype(jnp.float32)
    link_im = link_pair[1].astype(jnp.float32)
    spin_re = spinor[0].astype(jnp.float32)
    spin_im = spinor[1].astype(jnp.float32)
    out_re = []
    out_im = []
    for row in range(3):
        acc_re = None
        acc_im = None
        for col in range(3):
            if dagger:
                entry_re = link_re[col, row]
                entry_im = -link_im[col, row]
            else:
                entry_re = link_re[row, col]
                entry_im = link_im[row, col]
            part_re = entry_re * spin_re[:, col] - entry_im * spin_im[:, col]
            part_im = entry_re * spin_im[:, col] + entry_im * spin_re[:, col]
            acc_re = part_re if acc_re is None else acc_re + part_re
            acc_im = part_im if acc_im is None else acc_im + part_im
        out_re.append(acc_re)
        out_im.append(acc_im)
    return jnp.stack([jnp.stack(out_re, axis=1), jnp.stack(out_im, axis=1)])


def local_shift(values, direction, step):
    if direction == 1:
        return jnp.roll(values, -step * LX, axis=-1)
    column = lax.broadcasted_iota(jnp.int32, values.shape, values.ndim - 1) % LX
    edge = LX - 1 if step > 0 else 0
    return jnp.where(
        column == edge,
        jnp.roll(values, step * (LX - 1), axis=-1),
        jnp.roll(values, -step, axis=-1),
    )


def halo(block, axis, dim, step):
    size = block.shape[dim]
    if step > 0:
        edge = lax.slice_in_dim(block, 0, 1, axis=dim)
        inner = lax.slice_in_dim(block, 1, size, axis=dim)
        return jnp.concatenate([inner, shifted(edge, axis, -1)], axis=dim)
    edge = lax.slice_in_dim(block, size - 1, size, axis=dim)
    inner = lax.slice_in_dim(block, 0, size - 1, axis=dim)
    return jnp.concatenate([shifted(edge, axis, 1), inner], axis=dim)


def nested_project(wide, direction, sign):
    rows = [[], []]
    for slot in range(2):
        other = spin_perms[direction][slot]
        row_re, row_im = [], []
        for color in range(3):
            term_re, term_im = phase_mul(
                spin_real[direction][slot],
                spin_imag[direction][slot],
                wide[0][other][color],
                wide[1][other][color],
            )
            row_re.append(wide[0][slot][color] + sign * term_re)
            row_im.append(wide[1][slot][color] + sign * term_im)
        rows[0].append(row_re)
        rows[1].append(row_im)
    return rows


def nested_expand(half, direction, sign):
    rows = [[None] * 4, [None] * 4]
    for slot in range(2):
        other = spin_perms[direction][slot]
        rows[0][slot] = half[0][slot]
        rows[1][slot] = half[1][slot]
        pairs = [
            phase_mul(
                spin_real[direction][other],
                spin_imag[direction][other],
                half[0][slot][color],
                half[1][slot][color],
            )
            for color in range(3)
        ]
        rows[0][other] = [sign * pair[0] for pair in pairs]
        rows[1][other] = [sign * pair[1] for pair in pairs]
    return rows


def nested_mix(link, spinor, dagger):
    out = [[], []]
    for spin in range(len(spinor[0])):
        out_re, out_im = [], []
        for row in range(3):
            acc_re = None
            acc_im = None
            for col in range(3):
                if dagger:
                    entry_re = link[0][col][row]
                    entry_im = -link[1][col][row]
                else:
                    entry_re = link[0][row][col]
                    entry_im = link[1][row][col]
                spin_re = spinor[0][spin][col]
                spin_im = spinor[1][spin][col]
                part_re = entry_re * spin_re - entry_im * spin_im
                part_im = entry_re * spin_im + entry_im * spin_re
                acc_re = part_re if acc_re is None else acc_re + part_re
                acc_im = part_im if acc_im is None else acc_im + part_im
            out_re.append(acc_re)
            out_im.append(acc_im)
        out[0].append(out_re)
        out[1].append(out_im)
    return out


def nested_map(nested, fn):
    return [[[fn(value) for value in colors] for colors in spins] for spins in nested]


def nested_read(ref, spins):
    return [
        [[ref[(part * spins + spin) * 3 + color].astype(jnp.float32) for color in range(3)] for spin in range(spins)]
        for part in range(2)
    ]


def hop_kernel(v_ref, u_ref, az_ref, bz_ref, at_ref, bt_ref, out_ref):
    width = v_ref.shape[-1]
    wide = nested_read(v_ref, 4)
    column = lax.broadcasted_iota(jnp.int32, wide[0][0][0].shape, 1) % LX

    def link(mu):
        return [
            [[u_ref[mu, (part * 3 + row) * 3 + col].astype(jnp.float32) for col in range(3)] for row in range(3)]
            for part in range(2)
        ]

    def round_half(value):
        return value.astype(jnp.bfloat16).astype(jnp.float32)

    shifts_ahead = (
        lambda a: jnp.where(column == LX - 1, pltpu.roll(a, LX - 1, 1), pltpu.roll(a, width - 1, 1)),
        lambda a: pltpu.roll(a, width - LX, 1),
    )
    shifts_behind = (
        lambda a: jnp.where(column == 0, pltpu.roll(a, width - LX + 1, 1), pltpu.roll(a, 1, 1)),
        lambda a: pltpu.roll(a, LX, 1),
    )
    total = [[[None] * 3 for _ in range(4)] for _ in range(2)]

    def accumulate(term):
        for part in range(2):
            for spin in range(4):
                for color in range(3):
                    value = term[part][spin][color]
                    old = total[part][spin][color]
                    total[part][spin][color] = value if old is None else old + value

    for mu in range(4):
        links = link(mu)
        if mu < 2:
            ahead = nested_map(nested_project(wide, mu, -1.0), lambda a: shifts_ahead[mu](round_half(a)))
            back = nested_project(nested_mix(links, wide, True), mu, 1.0)
            behind = nested_map(back, lambda a: shifts_behind[mu](round_half(a)))
        else:
            ahead = nested_read(az_ref if mu == 2 else at_ref, 2)
            behind = nested_read(bz_ref if mu == 2 else bt_ref, 2)
        accumulate(nested_expand(nested_mix(links, ahead, False), mu, -1.0))
        accumulate(nested_expand(behind, mu, 1.0))
    for part in range(2):
        for spin in range(4):
            for color in range(3):
                out_ref[(part * 4 + spin) * 3 + color] = total[part][spin][color]


def hopping(spinor, gauge_links):
    wide = spinor.astype(jnp.float32)
    fwd_z = project(wide, 2, -1.0).astype(jnp.bfloat16)
    fwd_t = project(wide, 3, -1.0).astype(jnp.bfloat16)
    back_z = project(color_mix(gauge_links[2], spinor, True), 2, 1.0).astype(jnp.bfloat16)
    back_t = project(color_mix(gauge_links[3], spinor, True), 3, 1.0).astype(jnp.bfloat16)
    halves = [
        halo(fwd_z, GZ, 4, 1),
        halo(back_z, GZ, 4, -1),
        halo(fwd_t, "ta", 3, 1),
        halo(back_t, "ta", 3, -1),
    ]
    shape = spinor.shape
    rows = shape[3] * shape[4]
    width = shape[5]
    flat = [half.reshape(12, rows, width) for half in halves]
    links = gauge_links.reshape(4, 18, rows, width)
    total = pl.pallas_call(
        hop_kernel,
        out_shape=jax.ShapeDtypeStruct((24, rows, width), jnp.float32),
        in_specs=[pl.BlockSpec(memory_space=pltpu.VMEM)] * 6,
        out_specs=pl.BlockSpec(memory_space=pltpu.VMEM),
        cost_estimate=pl.CostEstimate(
            flops=24 * 1024 * rows * width // 8, bytes_accessed=2 * 160 * rows * width, transcendentals=0
        ),
    )(spinor.reshape(24, rows, width), links, *flat)
    return total.reshape(shape)


def shards(source, gauge_links, clover_diag, agg_map, prolong, coarse_inverse):
    highest = lax.Precision.HIGHEST
    diagonal = 4.0 + mass_shift + clover_diag
    source_wide = source.astype(jnp.float32)
    first_iter = source_wide / diagonal
    first_half = first_iter.astype(jnp.bfloat16)
    first_resid = source_wide - diagonal * first_iter + 0.5 * hopping(first_half, gauge_links)
    second_iter = first_iter + first_resid / diagonal
    second_half = second_iter.astype(jnp.bfloat16)
    second_resid = source_wide - diagonal * second_iter + 0.5 * hopping(second_half, gauge_links)
    resid_half = second_resid.astype(jnp.bfloat16)
    projected = jnp.einsum(
        "vrsctzn,rsctzn->vtzn", prolong, resid_half, preferred_element_type=jnp.float32
    )
    vectors = prolong.shape[0]
    labels = jnp.arange(NAGG, dtype=jnp.int32)
    member = (agg_map[None] == labels[:, None, None, None]).astype(jnp.bfloat16)
    high = projected.astype(jnp.bfloat16)
    rest = projected - high.astype(jnp.float32)
    middle = rest.astype(jnp.bfloat16)
    low = (rest - middle.astype(jnp.float32)).astype(jnp.bfloat16)
    partial_sum = None
    for piece in (high, middle, low):
        term = jnp.einsum("atzn,vtzn->av", member, piece, preferred_element_type=jnp.float32)
        partial_sum = term if partial_sum is None else partial_sum + term
    coarse_resid = lax.psum(lax.psum(partial_sum.reshape(-1), "gx"), "gy")
    own_rows = jnp.dot(coarse_inverse[0], coarse_resid, precision=highest)
    rows = own_rows.shape[0]
    place = (lax.axis_index("gy") * lax.axis_size("gx") + lax.axis_index("gx")) * rows
    padded = lax.dynamic_update_slice(
        jnp.zeros((rows * lax.axis_size("gy") * lax.axis_size("gx"),), jnp.bfloat16), own_rows.astype(jnp.bfloat16), (place,)
    )
    correction_half = lax.psum(lax.psum(padded, "gx"), "gy").reshape(NAGG, vectors)
    spread = jnp.einsum(
        "av,atzn->vtzn", correction_half, member, preferred_element_type=jnp.float32
    ).astype(jnp.bfloat16)
    smooth = jnp.einsum(
        "vrsctzn,vtzn->rsctzn", prolong, spread, preferred_element_type=jnp.float32
    )
    return second_iter + smooth


def solution(mesh):
    ta, gz = mesh.devices.shape
    grid = Mesh(mesh.devices.reshape(ta, 4, gz // 4), ("ta", "gy", "gx"))
    return jax.shard_map(
        shards,
        mesh=grid,
        in_specs=(
            P(None, None, None, "ta", GZ, None),
            P(None, None, None, None, "ta", GZ, None),
            P(None, None, "ta", GZ, None),
            P("ta", GZ, None),
            P(None, None, None, None, "ta", GZ, None),
            P("ta", GZ, None),
        ),
        out_specs=P(None, None, None, "ta", GZ, None),
        check_vma=False,
    )
```

```python
import functools

import jax
import jax.numpy as jnp
from jax import lax
from jax.experimental import pallas as pl
from jax.experimental.pallas import tpu as pltpu
from jax.sharding import Mesh, PartitionSpec as P

LX = 32
LY = 16
NAGG = 32


mass_shift = -0.4
spin_perms = ((3, 2, 1, 0), (3, 2, 1, 0), (2, 3, 0, 1), (2, 3, 0, 1))
spin_real = (
    (0.0, 0.0, 0.0, 0.0),
    (-1.0, 1.0, 1.0, -1.0),
    (0.0, 0.0, 0.0, 0.0),
    (1.0, 1.0, 1.0, 1.0),
)
spin_imag = (
    (-1.0, -1.0, 1.0, 1.0),
    (0.0, 0.0, 0.0, 0.0),
    (-1.0, 1.0, 1.0, -1.0),
    (0.0, 0.0, 0.0, 0.0),
)


GZ = ("gy", "gx")


def shifted(block, axis, distance):
    count = 1
    for name in axis if isinstance(axis, tuple) else (axis,):
        count *= lax.axis_size(name)
    devices = range(count)
    route = [((i - distance) % len(devices), i) for i in devices]
    return lax.ppermute(block, axis, route)


def phase_mul(coef_re, coef_im, value_re, value_im):
    if coef_im == 0.0:
        return (coef_re * value_re, coef_re * value_im)
    return (-coef_im * value_im, coef_im * value_re)


def project(wide, direction, sign):
    rows_re = []
    rows_im = []
    for slot in range(2):
        other = spin_perms[direction][slot]
        term_re, term_im = phase_mul(
            spin_real[direction][slot], spin_imag[direction][slot], wide[0, other], wide[1, other]
        )
        rows_re.append(wide[0, slot] + sign * term_re)
        rows_im.append(wide[1, slot] + sign * term_im)
    return jnp.stack([jnp.stack(rows_re), jnp.stack(rows_im)])


def expand(half, direction, sign):
    rows_re = [None] * 4
    rows_im = [None] * 4
    for slot in range(2):
        other = spin_perms[direction][slot]
        rows_re[slot] = half[0, slot]
        rows_im[slot] = half[1, slot]
        term_re, term_im = phase_mul(
            spin_real[direction][other], spin_imag[direction][other], half[0, slot], half[1, slot]
        )
        rows_re[other] = sign * term_re
        rows_im[other] = sign * term_im
    return jnp.stack([jnp.stack(rows_re), jnp.stack(rows_im)])


def color_mix(link_pair, spinor, dagger):
    link_re = link_pair[0].astype(jnp.float32)
    link_im = link_pair[1].astype(jnp.float32)
    spin_re = spinor[0].astype(jnp.float32)
    spin_im = spinor[1].astype(jnp.float32)
    out_re = []
    out_im = []
    for row in range(3):
        acc_re = None
        acc_im = None
        for col in range(3):
            if dagger:
                entry_re = link_re[col, row]
                entry_im = -link_im[col, row]
            else:
                entry_re = link_re[row, col]
                entry_im = link_im[row, col]
            part_re = entry_re * spin_re[:, col] - entry_im * spin_im[:, col]
            part_im = entry_re * spin_im[:, col] + entry_im * spin_re[:, col]
            acc_re = part_re if acc_re is None else acc_re + part_re
            acc_im = part_im if acc_im is None else acc_im + part_im
        out_re.append(acc_re)
        out_im.append(acc_im)
    return jnp.stack([jnp.stack(out_re, axis=1), jnp.stack(out_im, axis=1)])


def local_shift(values, direction, step):
    if direction == 1:
        return jnp.roll(values, -step * LX, axis=-1)
    column = lax.broadcasted_iota(jnp.int32, values.shape, values.ndim - 1) % LX
    edge = LX - 1 if step > 0 else 0
    return jnp.where(
        column == edge,
        jnp.roll(values, step * (LX - 1), axis=-1),
        jnp.roll(values, -step, axis=-1),
    )


def halo(block, axis, dim, step):
    size = block.shape[dim]
    if step > 0:
        edge = lax.slice_in_dim(block, 0, 1, axis=dim)
        inner = lax.slice_in_dim(block, 1, size, axis=dim)
        return jnp.concatenate([inner, shifted(edge, axis, -1)], axis=dim)
    edge = lax.slice_in_dim(block, size - 1, size, axis=dim)
    inner = lax.slice_in_dim(block, 0, size - 1, axis=dim)
    return jnp.concatenate([shifted(edge, axis, 1), inner], axis=dim)


def nested_project(wide, direction, sign):
    rows = [[], []]
    for slot in range(2):
        other = spin_perms[direction][slot]
        row_re, row_im = [], []
        for color in range(3):
            term_re, term_im = phase_mul(
                spin_real[direction][slot],
                spin_imag[direction][slot],
                wide[0][other][color],
                wide[1][other][color],
            )
            row_re.append(wide[0][slot][color] + sign * term_re)
            row_im.append(wide[1][slot][color] + sign * term_im)
        rows[0].append(row_re)
        rows[1].append(row_im)
    return rows


def nested_expand(half, direction, sign):
    rows = [[None] * 4, [None] * 4]
    for slot in range(2):
        other = spin_perms[direction][slot]
        rows[0][slot] = half[0][slot]
        rows[1][slot] = half[1][slot]
        pairs = [
            phase_mul(
                spin_real[direction][other],
                spin_imag[direction][other],
                half[0][slot][color],
                half[1][slot][color],
            )
            for color in range(3)
        ]
        rows[0][other] = [sign * pair[0] for pair in pairs]
        rows[1][other] = [sign * pair[1] for pair in pairs]
    return rows


def nested_mix(link, spinor, dagger):
    out = [[], []]
    for spin in range(len(spinor[0])):
        out_re, out_im = [], []
        for row in range(3):
            acc_re = None
            acc_im = None
            for col in range(3):
                if dagger:
                    entry_re = link[0][col][row]
                    entry_im = -link[1][col][row]
                else:
                    entry_re = link[0][row][col]
                    entry_im = link[1][row][col]
                spin_re = spinor[0][spin][col]
                spin_im = spinor[1][spin][col]
                part_re = entry_re * spin_re - entry_im * spin_im
                part_im = entry_re * spin_im + entry_im * spin_re
                acc_re = part_re if acc_re is None else acc_re + part_re
                acc_im = part_im if acc_im is None else acc_im + part_im
            out_re.append(acc_re)
            out_im.append(acc_im)
        out[0].append(out_re)
        out[1].append(out_im)
    return out


def nested_map(nested, fn):
    return [[[fn(value) for value in colors] for colors in spins] for spins in nested]


def nested_read(ref, spins):
    return [
        [[ref[(part * spins + spin) * 3 + color].astype(jnp.float32) for color in range(3)] for spin in range(spins)]
        for part in range(2)
    ]


def sweep_kernel(last, v_ref, u_ref, az_ref, bz_ref, at_ref, bt_ref, src_ref, clov_ref, it_ref, *out_refs):
    width = v_ref.shape[-1]
    wide = nested_read(v_ref, 4)
    column = lax.broadcasted_iota(jnp.int32, wide[0][0][0].shape, 1) % LX

    def link(mu):
        return [
            [[u_ref[mu, (part * 3 + row) * 3 + col].astype(jnp.float32) for col in range(3)] for row in range(3)]
            for part in range(2)
        ]

    def round_half(value):
        return value.astype(jnp.bfloat16).astype(jnp.float32)

    shifts_ahead = (
        lambda a: jnp.where(column == LX - 1, pltpu.roll(a, LX - 1, 1), pltpu.roll(a, width - 1, 1)),
        lambda a: pltpu.roll(a, width - LX, 1),
    )
    shifts_behind = (
        lambda a: jnp.where(column == 0, pltpu.roll(a, width - LX + 1, 1), pltpu.roll(a, 1, 1)),
        lambda a: pltpu.roll(a, LX, 1),
    )
    total = [[[None] * 3 for _ in range(4)] for _ in range(2)]

    def accumulate(term):
        for part in range(2):
            for spin in range(4):
                for color in range(3):
                    value = term[part][spin][color]
                    old = total[part][spin][color]
                    total[part][spin][color] = value if old is None else old + value

    for mu in range(4):
        links = link(mu)
        if mu < 2:
            ahead = nested_map(nested_project(wide, mu, -1.0), lambda a: shifts_ahead[mu](round_half(a)))
            back = nested_project(nested_mix(links, wide, True), mu, 1.0)
            behind = nested_map(back, lambda a: shifts_behind[mu](round_half(a)))
        else:
            ahead = nested_read(az_ref if mu == 2 else at_ref, 2)
            behind = nested_read(bz_ref if mu == 2 else bt_ref, 2)
        accumulate(nested_expand(nested_mix(links, ahead, False), mu, -1.0))
        accumulate(nested_expand(behind, mu, 1.0))
    half = [[[None] * 3 for _ in range(4)] for _ in range(2)]
    for part in range(2):
        for spin in range(4):
            for color in range(3):
                index = (part * 4 + spin) * 3 + color
                diagonal = 4.0 + mass_shift + clov_ref[spin * 3 + color]
                iterate = it_ref[index]
                resid = src_ref[index].astype(jnp.float32) - diagonal * iterate + 0.5 * total[part][spin][color]
                if last:
                    out_refs[0][index] = resid.astype(jnp.bfloat16)
                else:
                    new = iterate + resid / diagonal
                    out_refs[0][index] = new
                    rounded = new.astype(jnp.bfloat16)
                    out_refs[1][index] = rounded
                    half[part][spin][color] = rounded.astype(jnp.float32)
    if last:
        return
    sends = (
        nested_project(half, 2, -1.0),
        nested_project(half, 3, -1.0),
        nested_project(nested_mix(link(2), half, True), 2, 1.0),
        nested_project(nested_mix(link(3), half, True), 3, 1.0),
    )
    for ref, send in zip(out_refs[2:], sends):
        for part in range(2):
            for slot in range(2):
                for color in range(3):
                    ref[(part * 2 + slot) * 3 + color] = send[part][slot][color].astype(jnp.bfloat16)


def first_sends(spinor, gauge_links):
    wide = spinor.astype(jnp.float32)
    return (
        project(wide, 2, -1.0).astype(jnp.bfloat16),
        project(wide, 3, -1.0).astype(jnp.bfloat16),
        project(color_mix(gauge_links[2], spinor, True), 2, 1.0).astype(jnp.bfloat16),
        project(color_mix(gauge_links[3], spinor, True), 3, 1.0).astype(jnp.bfloat16),
    )


def sweep(last, spinor, gauge_links, sends, source, clover_diag, iterate):
    fwd_z, fwd_t, back_z, back_t = sends
    halves = [
        halo(fwd_z, GZ, 4, 1),
        halo(back_z, GZ, 4, -1),
        halo(fwd_t, "ta", 3, 1),
        halo(back_t, "ta", 3, -1),
    ]
    shape = spinor.shape
    rows = shape[3] * shape[4]
    width = shape[5]
    flat = [half.reshape(12, rows, width) for half in halves]
    links = gauge_links.reshape(4, 18, rows, width)
    full = jax.ShapeDtypeStruct((24, rows, width), jnp.float32)
    if last:
        out_shape = [full.update(dtype=jnp.bfloat16)]
    else:
        part = jax.ShapeDtypeStruct((12, rows, width), jnp.bfloat16)
        out_shape = [full, full.update(dtype=jnp.bfloat16), part, part, part, part]
    outs = pl.pallas_call(
        functools.partial(sweep_kernel, last),
        out_shape=out_shape,
        in_specs=[pl.BlockSpec(memory_space=pltpu.VMEM)] * 9,
        out_specs=[pl.BlockSpec(memory_space=pltpu.VMEM)] * len(out_shape),
        cost_estimate=pl.CostEstimate(
            flops=24 * 1200 * rows * width // 8, bytes_accessed=2 * 200 * rows * width, transcendentals=0
        ),
    )(
        spinor.reshape(24, rows, width),
        links,
        *flat,
        source.reshape(24, rows, width),
        clover_diag.reshape(12, rows, width),
        iterate.reshape(24, rows, width),
    )
    if last:
        return outs[0].reshape(shape)
    half_shape = (2, 2, 3) + shape[3:]
    return (
        outs[0].reshape(shape),
        outs[1].reshape(shape),
        tuple(out.reshape(half_shape) for out in outs[2:]),
    )


def shards(source, gauge_links, clover_diag, agg_map, prolong, coarse_inverse):
    highest = lax.Precision.HIGHEST
    diagonal = 4.0 + mass_shift + clover_diag
    source_wide = source.astype(jnp.float32)
    first_iter = source_wide / diagonal
    first_half = first_iter.astype(jnp.bfloat16)
    sends = first_sends(first_half, gauge_links)
    second_iter, second_half, sends = sweep(
        False, first_half, gauge_links, sends, source, clover_diag, first_iter
    )
    resid_half = sweep(True, second_half, gauge_links, sends, source, clover_diag, second_iter)
    projected = jnp.einsum(
        "vrsctzn,rsctzn->vtzn", prolong, resid_half, preferred_element_type=jnp.float32
    )
    vectors = prolong.shape[0]
    labels = jnp.arange(NAGG, dtype=jnp.int32)
    member = (agg_map[None] == labels[:, None, None, None]).astype(jnp.bfloat16)
    high = projected.astype(jnp.bfloat16)
    rest = projected - high.astype(jnp.float32)
    middle = rest.astype(jnp.bfloat16)
    low = (rest - middle.astype(jnp.float32)).astype(jnp.bfloat16)
    partial_sum = None
    for piece in (high, middle, low):
        term = jnp.einsum("atzn,vtzn->av", member, piece, preferred_element_type=jnp.float32)
        partial_sum = term if partial_sum is None else partial_sum + term
    coarse_resid = lax.psum(lax.psum(partial_sum.reshape(-1), "gx"), "gy")
    own_rows = jnp.dot(coarse_inverse[0], coarse_resid, precision=highest)
    rows = own_rows.shape[0]
    place = (lax.axis_index("gy") * lax.axis_size("gx") + lax.axis_index("gx")) * rows
    padded = lax.dynamic_update_slice(
        jnp.zeros((rows * lax.axis_size("gy") * lax.axis_size("gx"),), jnp.bfloat16), own_rows.astype(jnp.bfloat16), (place,)
    )
    correction_half = lax.psum(lax.psum(padded, "gx"), "gy").reshape(NAGG, vectors)
    spread = jnp.einsum(
        "av,atzn->vtzn", correction_half, member, preferred_element_type=jnp.float32
    ).astype(jnp.bfloat16)
    smooth = jnp.einsum(
        "vrsctzn,vtzn->rsctzn", prolong, spread, preferred_element_type=jnp.float32
    )
    return second_iter + smooth


def solution(mesh):
    ta, gz = mesh.devices.shape
    grid = Mesh(mesh.devices.reshape(ta, 4, gz // 4), ("ta", "gy", "gx"))
    return jax.shard_map(
        shards,
        mesh=grid,
        in_specs=(
            P(None, None, None, "ta", GZ, None),
            P(None, None, None, None, "ta", GZ, None),
            P(None, None, "ta", GZ, None),
            P("ta", GZ, None),
            P(None, None, None, None, "ta", GZ, None),
            P("ta", GZ, None),
        ),
        out_specs=P(None, None, None, "ta", GZ, None),
        check_vma=False,
    )
```

```python
import functools

import jax
import jax.numpy as jnp
from jax import lax
from jax.experimental import pallas as pl
from jax.experimental.pallas import tpu as pltpu
from jax.sharding import Mesh, PartitionSpec as P

LX = 32
LY = 16
NAGG = 32


mass_shift = -0.4
spin_perms = ((3, 2, 1, 0), (3, 2, 1, 0), (2, 3, 0, 1), (2, 3, 0, 1))
spin_real = (
    (0.0, 0.0, 0.0, 0.0),
    (-1.0, 1.0, 1.0, -1.0),
    (0.0, 0.0, 0.0, 0.0),
    (1.0, 1.0, 1.0, 1.0),
)
spin_imag = (
    (-1.0, -1.0, 1.0, 1.0),
    (0.0, 0.0, 0.0, 0.0),
    (-1.0, 1.0, 1.0, -1.0),
    (0.0, 0.0, 0.0, 0.0),
)


GZ = ("gy", "gx")


def shifted(block, axis, distance):
    count = 1
    for name in axis if isinstance(axis, tuple) else (axis,):
        count *= lax.axis_size(name)
    devices = range(count)
    route = [((i - distance) % len(devices), i) for i in devices]
    return lax.ppermute(block, axis, route)


def phase_mul(coef_re, coef_im, value_re, value_im):
    if coef_im == 0.0:
        return (coef_re * value_re, coef_re * value_im)
    return (-coef_im * value_im, coef_im * value_re)


def project(wide, direction, sign):
    rows_re = []
    rows_im = []
    for slot in range(2):
        other = spin_perms[direction][slot]
        term_re, term_im = phase_mul(
            spin_real[direction][slot], spin_imag[direction][slot], wide[0, other], wide[1, other]
        )
        rows_re.append(wide[0, slot] + sign * term_re)
        rows_im.append(wide[1, slot] + sign * term_im)
    return jnp.stack([jnp.stack(rows_re), jnp.stack(rows_im)])


def expand(half, direction, sign):
    rows_re = [None] * 4
    rows_im = [None] * 4
    for slot in range(2):
        other = spin_perms[direction][slot]
        rows_re[slot] = half[0, slot]
        rows_im[slot] = half[1, slot]
        term_re, term_im = phase_mul(
            spin_real[direction][other], spin_imag[direction][other], half[0, slot], half[1, slot]
        )
        rows_re[other] = sign * term_re
        rows_im[other] = sign * term_im
    return jnp.stack([jnp.stack(rows_re), jnp.stack(rows_im)])


def color_mix(link_pair, spinor, dagger):
    link_re = link_pair[0].astype(jnp.float32)
    link_im = link_pair[1].astype(jnp.float32)
    spin_re = spinor[0].astype(jnp.float32)
    spin_im = spinor[1].astype(jnp.float32)
    out_re = []
    out_im = []
    for row in range(3):
        acc_re = None
        acc_im = None
        for col in range(3):
            if dagger:
                entry_re = link_re[col, row]
                entry_im = -link_im[col, row]
            else:
                entry_re = link_re[row, col]
                entry_im = link_im[row, col]
            part_re = entry_re * spin_re[:, col] - entry_im * spin_im[:, col]
            part_im = entry_re * spin_im[:, col] + entry_im * spin_re[:, col]
            acc_re = part_re if acc_re is None else acc_re + part_re
            acc_im = part_im if acc_im is None else acc_im + part_im
        out_re.append(acc_re)
        out_im.append(acc_im)
    return jnp.stack([jnp.stack(out_re, axis=1), jnp.stack(out_im, axis=1)])


def local_shift(values, direction, step):
    if direction == 1:
        return jnp.roll(values, -step * LX, axis=-1)
    column = lax.broadcasted_iota(jnp.int32, values.shape, values.ndim - 1) % LX
    edge = LX - 1 if step > 0 else 0
    return jnp.where(
        column == edge,
        jnp.roll(values, step * (LX - 1), axis=-1),
        jnp.roll(values, -step, axis=-1),
    )


def halo(block, axis, dim, step):
    size = block.shape[dim]
    if step > 0:
        edge = lax.slice_in_dim(block, 0, 1, axis=dim)
        inner = lax.slice_in_dim(block, 1, size, axis=dim)
        return jnp.concatenate([inner, shifted(edge, axis, -1)], axis=dim)
    edge = lax.slice_in_dim(block, size - 1, size, axis=dim)
    inner = lax.slice_in_dim(block, 0, size - 1, axis=dim)
    return jnp.concatenate([shifted(edge, axis, 1), inner], axis=dim)


def nested_project(wide, direction, sign):
    rows = [[], []]
    for slot in range(2):
        other = spin_perms[direction][slot]
        row_re, row_im = [], []
        for color in range(3):
            term_re, term_im = phase_mul(
                spin_real[direction][slot],
                spin_imag[direction][slot],
                wide[0][other][color],
                wide[1][other][color],
            )
            row_re.append(wide[0][slot][color] + sign * term_re)
            row_im.append(wide[1][slot][color] + sign * term_im)
        rows[0].append(row_re)
        rows[1].append(row_im)
    return rows


def nested_expand(half, direction, sign):
    rows = [[None] * 4, [None] * 4]
    for slot in range(2):
        other = spin_perms[direction][slot]
        rows[0][slot] = half[0][slot]
        rows[1][slot] = half[1][slot]
        pairs = [
            phase_mul(
                spin_real[direction][other],
                spin_imag[direction][other],
                half[0][slot][color],
                half[1][slot][color],
            )
            for color in range(3)
        ]
        rows[0][other] = [sign * pair[0] for pair in pairs]
        rows[1][other] = [sign * pair[1] for pair in pairs]
    return rows


def nested_mix(link, spinor, dagger):
    out = [[], []]
    for spin in range(len(spinor[0])):
        out_re, out_im = [], []
        for row in range(3):
            acc_re = None
            acc_im = None
            for col in range(3):
                if dagger:
                    entry_re = link[0][col][row]
                    entry_im = -link[1][col][row]
                else:
                    entry_re = link[0][row][col]
                    entry_im = link[1][row][col]
                spin_re = spinor[0][spin][col]
                spin_im = spinor[1][spin][col]
                part_re = entry_re * spin_re - entry_im * spin_im
                part_im = entry_re * spin_im + entry_im * spin_re
                acc_re = part_re if acc_re is None else acc_re + part_re
                acc_im = part_im if acc_im is None else acc_im + part_im
            out_re.append(acc_re)
            out_im.append(acc_im)
        out[0].append(out_re)
        out[1].append(out_im)
    return out


def nested_map(nested, fn):
    return [[[fn(value) for value in colors] for colors in spins] for spins in nested]


def nested_read(ref, spins):
    return [
        [[ref[(part * spins + spin) * 3 + color].astype(jnp.float32) for color in range(3)] for spin in range(spins)]
        for part in range(2)
    ]


def sweep_kernel(last, v_ref, u_ref, az_ref, bz_ref, at_ref, bt_ref, src_ref, clov_ref, it_ref, *out_refs):
    width = v_ref.shape[-1]
    wide = nested_read(v_ref, 4)
    column = lax.broadcasted_iota(jnp.int32, wide[0][0][0].shape, 1) % LX

    def link(mu):
        return [
            [[u_ref[mu, (part * 3 + row) * 3 + col].astype(jnp.float32) for col in range(3)] for row in range(3)]
            for part in range(2)
        ]

    def round_half(value):
        return value.astype(jnp.bfloat16).astype(jnp.float32)

    shifts_ahead = (
        lambda a: jnp.where(column == LX - 1, pltpu.roll(a, LX - 1, 1), pltpu.roll(a, width - 1, 1)),
        lambda a: pltpu.roll(a, width - LX, 1),
    )
    shifts_behind = (
        lambda a: jnp.where(column == 0, pltpu.roll(a, width - LX + 1, 1), pltpu.roll(a, 1, 1)),
        lambda a: pltpu.roll(a, LX, 1),
    )
    total = [[[None] * 3 for _ in range(4)] for _ in range(2)]

    def accumulate(term):
        for part in range(2):
            for spin in range(4):
                for color in range(3):
                    value = term[part][spin][color]
                    old = total[part][spin][color]
                    total[part][spin][color] = value if old is None else old + value

    for mu in range(4):
        links = link(mu)
        if mu < 2:
            ahead = nested_map(nested_project(wide, mu, -1.0), lambda a: shifts_ahead[mu](round_half(a)))
            back = nested_project(nested_mix(links, wide, True), mu, 1.0)
            behind = nested_map(back, lambda a: shifts_behind[mu](round_half(a)))
        else:
            ahead = nested_read(az_ref if mu == 2 else at_ref, 2)
            behind = nested_read(bz_ref if mu == 2 else bt_ref, 2)
        accumulate(nested_expand(nested_mix(links, ahead, False), mu, -1.0))
        accumulate(nested_expand(behind, mu, 1.0))
    half = [[[None] * 3 for _ in range(4)] for _ in range(2)]
    for part in range(2):
        for spin in range(4):
            for color in range(3):
                index = (part * 4 + spin) * 3 + color
                diagonal = 4.0 + mass_shift + clov_ref[spin * 3 + color]
                iterate = it_ref[index]
                resid = src_ref[index].astype(jnp.float32) - diagonal * iterate + 0.5 * total[part][spin][color]
                if last:
                    out_refs[0][index] = resid.astype(jnp.bfloat16)
                else:
                    new = iterate + resid / diagonal
                    out_refs[0][index] = new
                    rounded = new.astype(jnp.bfloat16)
                    out_refs[1][index] = rounded
                    half[part][spin][color] = rounded.astype(jnp.float32)
    if len(out_refs) < 3:
        return
    sends = (
        nested_project(half, 2, -1.0),
        nested_project(half, 3, -1.0),
        nested_project(nested_mix(link(2), half, True), 2, 1.0),
        nested_project(nested_mix(link(3), half, True), 3, 1.0),
    )
    for ref, send in zip(out_refs[2:], sends):
        for part in range(2):
            for slot in range(2):
                for color in range(3):
                    ref[(part * 2 + slot) * 3 + color] = send[part][slot][color].astype(jnp.bfloat16)


def first_sends(spinor, gauge_links):
    wide = spinor.astype(jnp.float32)
    return (
        project(wide, 2, -1.0).astype(jnp.bfloat16),
        project(wide, 3, -1.0).astype(jnp.bfloat16),
        project(color_mix(gauge_links[2], spinor, True), 2, 1.0).astype(jnp.bfloat16),
        project(color_mix(gauge_links[3], spinor, True), 3, 1.0).astype(jnp.bfloat16),
    )


def sweep(last, spinor, gauge_links, sends, source, clover_diag, iterate):
    fwd_z, fwd_t, back_z, back_t = sends
    halves = [
        halo(fwd_z, GZ, 4, 1),
        halo(back_z, GZ, 4, -1),
        halo(fwd_t, "ta", 3, 1),
        halo(back_t, "ta", 3, -1),
    ]
    shape = spinor.shape
    rows = shape[3] * shape[4]
    width = shape[5]
    flat = [half.reshape(12, rows, width) for half in halves]
    links = gauge_links.reshape(4, 18, rows, width)
    full = jax.ShapeDtypeStruct((24, rows, width), jnp.float32)
    if last:
        out_shape = [full.update(dtype=jnp.bfloat16)]
    else:
        out_shape = [full, full.update(dtype=jnp.bfloat16)]
    outs = pl.pallas_call(
        functools.partial(sweep_kernel, last),
        out_shape=out_shape,
        in_specs=[pl.BlockSpec(memory_space=pltpu.VMEM)] * 9,
        out_specs=[pl.BlockSpec(memory_space=pltpu.VMEM)] * len(out_shape),
        cost_estimate=pl.CostEstimate(
            flops=24 * 1200 * rows * width // 8, bytes_accessed=2 * 200 * rows * width, transcendentals=0
        ),
    )(
        spinor.reshape(24, rows, width),
        links,
        *flat,
        source.reshape(24, rows, width),
        clover_diag.reshape(12, rows, width),
        iterate.reshape(24, rows, width),
    )
    if last:
        return outs[0].reshape(shape)
    second_half = outs[1].reshape(shape)
    return outs[0].reshape(shape), second_half, first_sends(second_half, gauge_links)


def shards(source, gauge_links, clover_diag, agg_map, prolong, coarse_inverse):
    highest = lax.Precision.HIGHEST
    diagonal = 4.0 + mass_shift + clover_diag
    source_wide = source.astype(jnp.float32)
    first_iter = source_wide / diagonal
    first_half = first_iter.astype(jnp.bfloat16)
    sends = first_sends(first_half, gauge_links)
    second_iter, second_half, sends = sweep(
        False, first_half, gauge_links, sends, source, clover_diag, first_iter
    )
    resid_half = sweep(True, second_half, gauge_links, sends, source, clover_diag, second_iter)
    projected = jnp.einsum(
        "vrsctzn,rsctzn->vtzn", prolong, resid_half, preferred_element_type=jnp.float32
    )
    vectors = prolong.shape[0]
    labels = jnp.arange(NAGG, dtype=jnp.int32)
    member = (agg_map[None] == labels[:, None, None, None]).astype(jnp.bfloat16)
    high = projected.astype(jnp.bfloat16)
    rest = projected - high.astype(jnp.float32)
    middle = rest.astype(jnp.bfloat16)
    low = (rest - middle.astype(jnp.float32)).astype(jnp.bfloat16)
    partial_sum = None
    for piece in (high, middle, low):
        term = jnp.einsum("atzn,vtzn->av", member, piece, preferred_element_type=jnp.float32)
        partial_sum = term if partial_sum is None else partial_sum + term
    coarse_resid = lax.psum(lax.psum(partial_sum.reshape(-1), "gx"), "gy")
    own_rows = jnp.dot(coarse_inverse[0], coarse_resid, precision=highest)
    rows = own_rows.shape[0]
    place = (lax.axis_index("gy") * lax.axis_size("gx") + lax.axis_index("gx")) * rows
    padded = lax.dynamic_update_slice(
        jnp.zeros((rows * lax.axis_size("gy") * lax.axis_size("gx"),), jnp.bfloat16), own_rows.astype(jnp.bfloat16), (place,)
    )
    correction_half = lax.psum(lax.psum(padded, "gx"), "gy").reshape(NAGG, vectors)
    spread = jnp.einsum(
        "av,atzn->vtzn", correction_half, member, preferred_element_type=jnp.float32
    ).astype(jnp.bfloat16)
    smooth = jnp.einsum(
        "vrsctzn,vtzn->rsctzn", prolong, spread, preferred_element_type=jnp.float32
    )
    return second_iter + smooth


def solution(mesh):
    ta, gz = mesh.devices.shape
    grid = Mesh(mesh.devices.reshape(ta, 4, gz // 4), ("ta", "gy", "gx"))
    return jax.shard_map(
        shards,
        mesh=grid,
        in_specs=(
            P(None, None, None, "ta", GZ, None),
            P(None, None, None, None, "ta", GZ, None),
            P(None, None, "ta", GZ, None),
            P("ta", GZ, None),
            P(None, None, None, None, "ta", GZ, None),
            P("ta", GZ, None),
        ),
        out_specs=P(None, None, None, "ta", GZ, None),
        check_vma=False,
    )
```
